768 devices in a mesh: fsdp: 12 (over z), tensor: 64 (over y, x, core).
Axes of the slice: x: 4, y: 8, z: 12, core: 2. Of those that a mesh axis runs over, the one named last changes fastest.
Arguments:
- momentum: float32 [1536, 24576], P('fsdp', 'tensor'), may hold values from -6 to 6
- gradient: bfloat16 [1536, 24576], P('fsdp', 'tensor'), may hold values from -6 to 6
- weight: bfloat16 [1536, 24576], P('fsdp', 'tensor'), may hold values from -6 to 6
- basis: float32 [24576, 512], P('tensor'), may hold values from -0.0390625 to 0.0390625
Outputs:
- new_momentum: float32 [1536, 24576], P('fsdp', 'tensor')
- new_basis: float32 [24576, 512], P('tensor')
- new_weight: bfloat16 [1536, 24576], P('fsdp', 'tensor')
The draws below stay inside these ranges and needn't reach their ends.
All inputs are finite; a program needn't handle non-finite values.
Results may differ from the reference program's by a relative error of at most 0.001.
Values sent between devices are 32-bit elements; how exact they have to be, the bound alone decides.
No kernel may reach another device: no remote copies, remote signals or barrier semaphores. Data moves between devices by JAX's collectives and lax.ppermute only.
A program may use at most 32 MiB of HBM per device.

```python
import jax
import jax.numpy as jnp
from jax import lax

RANK = 512
ROWS = 1536
COLS = 24576


def steps_of(key, extent, pieces, low, high):
    gain = 1.0
    for position, parts in pieces:
        steps = jax.random.uniform(jax.random.fold_in(jax.random.fold_in(key, 6), position), (parts,), jnp.float32, low / len(pieces), high / len(pieces))
        gain = gain * jnp.repeat(jnp.exp(steps), extent[position] // parts).reshape((-1,) + (1,) * (len(extent) - 1 - position))
    return gain


def scatter_about(rng, extent, width, most, cuts=(), held_as=jnp.bfloat16):
    array = width * jax.random.normal(rng, extent, jnp.float32)
    if cuts:
        array = array * steps_of(rng, extent, cuts, -0.22, 0.18)
    return jnp.clip(array, -most, most).astype(held_as)


def setup_inputs(seed: int = 0) -> dict:
    streams_of = jax.random.split(jax.random.key(seed), 5)
    return {
        "momentum": scatter_about(streams_of[0], (ROWS, COLS), 1.0, 6.0, ((0, 12), (1, 64)), jnp.float32),
        "gradient": scatter_about(streams_of[1], (ROWS, COLS), 1.0, 6.0, ((0, 12), (1, 64))),
        "weight": scatter_about(streams_of[2], (ROWS, COLS), 1.0, 6.0, ((0, 12), (1, 64))),
        "basis": scatter_about(streams_of[3], (COLS, RANK), COLS ** -0.5, 0.0390625, ((0, 64),), jnp.float32),
    }


def reference(momentum, gradient, weight, basis):
    highest = lax.Precision.HIGHEST
    buffer = momentum + gradient.astype(jnp.float32)
    panel = jnp.dot(buffer, basis, precision=highest)
    gram_matrix = jnp.dot(panel.T, panel, precision=highest)
    factor = jnp.linalg.cholesky(gram_matrix)
    orthonormal = lax.linalg.triangular_solve(factor, panel, left_side=False, lower=True, transpose_a=True)
    right_factor = jnp.dot(buffer.T, orthonormal, precision=highest)
    new_momentum = buffer - 0.1 * jnp.dot(orthonormal, right_factor.T, precision=highest)
    col_sumsq = lax.optimization_barrier(jnp.sum(right_factor * right_factor, axis=0))
    new_basis = right_factor / jnp.sqrt(col_sumsq + 1e-06)
    step_scale = 0.2 * jnp.sqrt(jnp.float32(ROWS * COLS / RANK))
    update = jnp.dot(orthonormal, new_basis.T, precision=highest)
    new_weight = (weight.astype(jnp.float32) - step_scale * update).astype(jnp.bfloat16)
    return (new_momentum, new_basis, new_weight)
```

```python
import jax
import jax.numpy as jnp
from jax import lax
from jax.sharding import PartitionSpec as P


def xor_psum(x, axis, size):
    step = 1
    while step < size:
        x = x + lax.ppermute(x, axis, [(i, i ^ step) for i in range(size)])
        step *= 2
    return x


def local(momentum, gradient, weight, basis):
    highest = lax.Precision.HIGHEST
    rank = basis.shape[1]
    buffer = momentum + gradient.astype(jnp.float32)
    panel_part = jnp.dot(buffer, basis, precision=highest)
    tensor_size = lax.axis_size("tensor")
    panel_full = xor_psum(panel_part, "tensor", tensor_size)
    gram_part = jnp.dot(panel_full.T, panel_full, precision=highest)
    cross_part = jnp.dot(buffer.T, panel_full, precision=highest)
    merged = lax.psum(jnp.concatenate([gram_part, cross_part], axis=0), "fsdp")
    gram_matrix = merged[:rank]
    cross = merged[rank:]
    factor = jnp.linalg.cholesky(gram_matrix)
    rows = panel_full.shape[0]
    solved = lax.linalg.triangular_solve(
        factor, jnp.concatenate([panel_full, cross], axis=0), left_side=False, lower=True, transpose_a=True
    )
    orthonormal = solved[:rows]
    right_factor = solved[rows:]
    col_sumsq = xor_psum(jnp.sum(right_factor * right_factor, axis=0), "tensor", tensor_size)
    new_basis = right_factor / jnp.sqrt(col_sumsq + 1e-06)
    new_momentum = buffer - 0.1 * jnp.dot(orthonormal, right_factor.T, precision=highest)
    total_rows = buffer.shape[0] * lax.axis_size("fsdp")
    total_cols = buffer.shape[1] * lax.axis_size("tensor")
    step_scale = 0.2 * jnp.sqrt(jnp.float32(total_rows * total_cols / basis.shape[1]))
    update = jnp.dot(orthonormal, new_basis.T, precision=highest)
    new_weight = (weight.astype(jnp.float32) - step_scale * update).astype(jnp.bfloat16)
    return (new_momentum, new_basis, new_weight)


def solution(mesh):
    placed = (P("fsdp", "tensor"), P("fsdp", "tensor"), P("fsdp", "tensor"), P("tensor", None))
    return jax.shard_map(
        local,
        mesh=mesh,
        in_specs=placed,
        out_specs=(P("fsdp", "tensor"), P("tensor", None), P("fsdp", "tensor")),
        check_vma=False,
    )
```

```python
import jax
import jax.numpy as jnp
from jax import lax
from jax.sharding import PartitionSpec as P


def scatter_gather_psum(x, axis, size):
    chunks = x.reshape(size, -1, 128)
    mine = jnp.sum(lax.all_to_all(chunks, axis, 0, 0, tiled=False), axis=0)
    spread = jnp.broadcast_to(mine[None], chunks.shape)
    return lax.all_to_all(spread, axis, 0, 0, tiled=False).reshape(x.shape)


def gather_psum(x, axis, size):
    copies = jnp.broadcast_to(x[None], (size,) + x.shape)
    return jnp.sum(lax.all_to_all(copies, axis, 0, 0, tiled=False), axis=0)


def local(momentum, gradient, weight, basis):
    highest = lax.Precision.HIGHEST
    rank = basis.shape[1]
    buffer = momentum + gradient.astype(jnp.float32)
    panel_part = jnp.dot(buffer, basis, precision=highest)
    tensor_size = lax.axis_size("tensor")
    panel_full = scatter_gather_psum(panel_part, "tensor", tensor_size)
    gram_part = jnp.dot(panel_full.T, panel_full, precision=highest)
    cross_part = jnp.dot(buffer.T, panel_full, precision=highest)
    merged = lax.psum(jnp.concatenate([gram_part, cross_part], axis=0), "fsdp")
    gram_matrix = merged[:rank]
    cross = merged[rank:]
    factor = jnp.linalg.cholesky(gram_matrix)
    rows = panel_full.shape[0]
    solved = lax.linalg.triangular_solve(
        factor, jnp.concatenate([panel_full, cross], axis=0), left_side=False, lower=True, transpose_a=True
    )
    orthonormal = solved[:rows]
    right_factor = solved[rows:]
    col_sumsq = gather_psum(jnp.sum(right_factor * right_factor, axis=0), "tensor", tensor_size)
    new_basis = right_factor / jnp.sqrt(col_sumsq + 1e-06)
    new_momentum = buffer - 0.1 * jnp.dot(orthonormal, right_factor.T, precision=highest)
    total_rows = buffer.shape[0] * lax.axis_size("fsdp")
    total_cols = buffer.shape[1] * lax.axis_size("tensor")
    step_scale = 0.2 * jnp.sqrt(jnp.float32(total_rows * total_cols / basis.shape[1]))
    update = jnp.dot(orthonormal, new_basis.T, precision=highest)
    new_weight = (weight.astype(jnp.float32) - step_scale * update).astype(jnp.bfloat16)
    return (new_momentum, new_basis, new_weight)


def solution(mesh):
    placed = (P("fsdp", "tensor"), P("fsdp", "tensor"), P("fsdp", "tensor"), P("tensor", None))
    return jax.shard_map(
        local,
        mesh=mesh,
        in_specs=placed,
        out_specs=(P("fsdp", "tensor"), P("tensor", None), P("fsdp", "tensor")),
        check_vma=False,
    )
```

```python
import jax
import jax.numpy as jnp
from jax import lax
from jax.sharding import PartitionSpec as P


def scatter_gather_psum(x, axis, size):
    chunks = x.reshape(size, -1, 128)
    mine = jnp.sum(lax.all_to_all(chunks, axis, 0, 0, tiled=False), axis=0)
    spread = jnp.broadcast_to(mine[None], chunks.shape)
    return lax.all_to_all(spread, axis, 0, 0, tiled=False).reshape(x.shape)


def padded_scatter_gather_psum(x, axis, size):
    flat = x.reshape(-1)
    chunk = size * 8 * 128
    padded = jnp.pad(flat, (0, (-flat.shape[0]) % chunk))
    summed = scatter_gather_psum(padded.reshape(-1, 128), axis, size)
    return summed.reshape(-1)[: flat.shape[0]].reshape(x.shape)


def lower_blocks(matrix, block):
    count = matrix.shape[0] // block
    return jnp.stack([matrix[i * block:(i + 1) * block, j * block:(j + 1) * block] for i in range(count) for j in range(i + 1)])


def symmetric_from_lower_blocks(blocks, count):
    block = blocks.shape[-1]
    index = {}
    for i in range(count):
        for j in range(i + 1):
            index[(i, j)] = len(index)
    rows = []
    for i in range(count):
        row = [blocks[index[(i, j)]] if j <= i else blocks[index[(j, i)]].T for j in range(count)]
        rows.append(jnp.concatenate(row, axis=1))
    return jnp.concatenate(rows, axis=0)


def gather_psum(x, axis, size):
    copies = jnp.broadcast_to(x[None], (size,) + x.shape)
    return jnp.sum(lax.all_to_all(copies, axis, 0, 0, tiled=False), axis=0)


def local(momentum, gradient, weight, basis):
    highest = lax.Precision.HIGHEST
    rank = basis.shape[1]
    buffer = momentum + gradient.astype(jnp.float32)
    panel_part = jnp.dot(buffer, basis, precision=highest)
    tensor_size = lax.axis_size("tensor")
    panel_full = scatter_gather_psum(panel_part, "tensor", tensor_size)
    gram_part = jnp.dot(panel_full.T, panel_full, precision=highest)
    block = 128
    fsdp_size = lax.axis_size("fsdp")
    gram_blocks = padded_scatter_gather_psum(lower_blocks(gram_part, block), "fsdp", fsdp_size)
    cross = padded_scatter_gather_psum(jnp.dot(buffer.T, panel_full, precision=highest), "fsdp", fsdp_size)
    gram_matrix = symmetric_from_lower_blocks(gram_blocks, rank // block)
    factor = jnp.linalg.cholesky(gram_matrix)
    rows = panel_full.shape[0]
    solved = lax.linalg.triangular_solve(
        factor, jnp.concatenate([panel_full, cross], axis=0), left_side=False, lower=True, transpose_a=True
    )
    orthonormal = solved[:rows]
    right_factor = solved[rows:]
    col_sumsq = gather_psum(jnp.sum(right_factor * right_factor, axis=0), "tensor", tensor_size)
    new_basis = right_factor / jnp.sqrt(col_sumsq + 1e-06)
    new_momentum = buffer - 0.1 * jnp.dot(orthonormal, right_factor.T, precision=highest)
    total_rows = buffer.shape[0] * lax.axis_size("fsdp")
    total_cols = buffer.shape[1] * lax.axis_size("tensor")
    step_scale = 0.2 * jnp.sqrt(jnp.float32(total_rows * total_cols / basis.shape[1]))
    update = jnp.dot(orthonormal, new_basis.T, precision=highest)
    new_weight = (weight.astype(jnp.float32) - step_scale * update).astype(jnp.bfloat16)
    return (new_momentum, new_basis, new_weight)


def solution(mesh):
    placed = (P("fsdp", "tensor"), P("fsdp", "tensor"), P("fsdp", "tensor"), P("tensor", None))
    return jax.shard_map(
        local,
        mesh=mesh,
        in_specs=placed,
        out_specs=(P("fsdp", "tensor"), P("tensor", None), P("fsdp", "tensor")),
        check_vma=False,
    )
```

```python
import jax
import jax.numpy as jnp
from jax import lax
from jax.sharding import PartitionSpec as P


def scatter_gather_psum(x, axis, size):
    chunks = x.reshape(size, -1, 128)
    mine = jnp.sum(lax.all_to_all(chunks, axis, 0, 0, tiled=False), axis=0)
    spread = jnp.broadcast_to(mine[None], chunks.shape)
    return lax.all_to_all(spread, axis, 0, 0, tiled=False).reshape(x.shape)


def padded_scatter_gather_psum(x, axis, size):
    flat = x.reshape(-1)
    chunk = size * 8 * 128
    padded = jnp.pad(flat, (0, (-flat.shape[0]) % chunk))
    summed = scatter_gather_psum(padded.reshape(-1, 128), axis, size)
    return summed.reshape(-1)[: flat.shape[0]].reshape(x.shape)


def lower_blocks(matrix, block):
    count = matrix.shape[0] // block
    return jnp.stack([matrix[i * block:(i + 1) * block, j * block:(j + 1) * block] for i in range(count) for j in range(i + 1)])


def symmetric_from_lower_blocks(blocks, count):
    block = blocks.shape[-1]
    index = {}
    for i in range(count):
        for j in range(i + 1):
            index[(i, j)] = len(index)
    rows = []
    for i in range(count):
        row = [blocks[index[(i, j)]] if j <= i else blocks[index[(j, i)]].T for j in range(count)]
        rows.append(jnp.concatenate(row, axis=1))
    return jnp.concatenate(rows, axis=0)


def gather_psum(x, axis, size):
    copies = jnp.broadcast_to(x[None], (size,) + x.shape)
    return jnp.sum(lax.all_to_all(copies, axis, 0, 0, tiled=False), axis=0)


def local(momentum, gradient, weight, basis):
    highest = lax.Precision.HIGHEST
    rank = basis.shape[1]
    buffer = momentum + gradient.astype(jnp.float32)
    panel_part = jnp.dot(buffer, basis, precision=highest)
    tensor_size = lax.axis_size("tensor")
    panel_full = scatter_gather_psum(panel_part, "tensor", tensor_size)
    gram_part = jnp.dot(panel_full.T, panel_full, precision=highest)
    block = 128
    fsdp_size = lax.axis_size("fsdp")
    gram_blocks = padded_scatter_gather_psum(lower_blocks(gram_part, block), "fsdp", fsdp_size)
    cross_part, gram_blocks = lax.optimization_barrier(
        (jnp.dot(buffer.T, panel_full, precision=highest), gram_blocks)
    )
    cross = padded_scatter_gather_psum(cross_part, "fsdp", fsdp_size)
    gram_matrix = symmetric_from_lower_blocks(gram_blocks, rank // block)
    factor = jnp.linalg.cholesky(gram_matrix)
    rows = panel_full.shape[0]
    solved = lax.linalg.triangular_solve(
        factor, jnp.concatenate([panel_full, cross], axis=0), left_side=False, lower=True, transpose_a=True
    )
    orthonormal = solved[:rows]
    right_factor = solved[rows:]
    col_sumsq = gather_psum(jnp.sum(right_factor * right_factor, axis=0), "tensor", tensor_size)
    new_basis = right_factor / jnp.sqrt(col_sumsq + 1e-06)
    new_momentum = buffer - 0.1 * jnp.dot(orthonormal, right_factor.T, precision=highest)
    total_rows = buffer.shape[0] * lax.axis_size("fsdp")
    total_cols = buffer.shape[1] * lax.axis_size("tensor")
    step_scale = 0.2 * jnp.sqrt(jnp.float32(total_rows * total_cols / basis.shape[1]))
    update = jnp.dot(orthonormal, new_basis.T, precision=highest)
    new_weight = (weight.astype(jnp.float32) - step_scale * update).astype(jnp.bfloat16)
    return (new_momentum, new_basis, new_weight)


def solution(mesh):
    placed = (P("fsdp", "tensor"), P("fsdp", "tensor"), P("fsdp", "tensor"), P("tensor", None))
    return jax.shard_map(
        local,
        mesh=mesh,
        in_specs=placed,
        out_specs=(P("fsdp", "tensor"), P("tensor", None), P("fsdp", "tensor")),
        check_vma=False,
    )
```

```python
import jax
import jax.numpy as jnp
from jax import lax
from jax.sharding import PartitionSpec as P


def scatter_gather_psum(x, axis, size):
    chunks = x.reshape(size, -1, 128)
    mine = jnp.sum(lax.all_to_all(chunks, axis, 0, 0, tiled=False), axis=0)
    spread = jnp.broadcast_to(mine[None], chunks.shape)
    return lax.all_to_all(spread, axis, 0, 0, tiled=False).reshape(x.shape)


def padded_scatter_gather_psum(x, axis, size):
    flat = x.reshape(-1)
    chunk = size * 8 * 128
    padded = jnp.pad(flat, (0, (-flat.shape[0]) % chunk))
    summed = scatter_gather_psum(padded.reshape(-1, 128), axis, size)
    return summed.reshape(-1)[: flat.shape[0]].reshape(x.shape)


def lower_blocks(matrix, block):
    count = matrix.shape[0] // block
    return jnp.stack([matrix[i * block:(i + 1) * block, j * block:(j + 1) * block] for i in range(count) for j in range(i + 1)])


def symmetric_from_lower_blocks(blocks, count):
    block = blocks.shape[-1]
    index = {}
    for i in range(count):
        for j in range(i + 1):
            index[(i, j)] = len(index)
    rows = []
    for i in range(count):
        row = [blocks[index[(i, j)]] if j <= i else blocks[index[(j, i)]].T for j in range(count)]
        rows.append(jnp.concatenate(row, axis=1))
    return jnp.concatenate(rows, axis=0)


def lower_inverse(factor):
    size = factor.shape[0]
    levels = [factor[None]]
    while levels[-1].shape[-1] > 1:
        blocks = levels[-1]
        half = blocks.shape[-1] // 2
        pair = jnp.stack([blocks[:, :half, :half], blocks[:, half:, half:]], axis=1)
        levels.append(pair.reshape(-1, half, half))
    inverse = 1.0 / levels[-1]
    for blocks in reversed(levels[:-1]):
        width = blocks.shape[-1] // 2
        upper = inverse[0::2]
        lower = inverse[1::2]
        corner = blocks[:, width:, :width]
        off = -jnp.matmul(jnp.matmul(lower, corner, precision=lax.Precision.HIGHEST), upper, precision=lax.Precision.HIGHEST)
        top = jnp.concatenate([upper, jnp.zeros_like(upper)], axis=2)
        bottom = jnp.concatenate([off, lower], axis=2)
        inverse = jnp.concatenate([top, bottom], axis=1)
    return inverse[0]


def gather_psum(x, axis, size):
    copies = jnp.broadcast_to(x[None], (size,) + x.shape)
    return jnp.sum(lax.all_to_all(copies, axis, 0, 0, tiled=False), axis=0)


def local(momentum, gradient, weight, basis):
    highest = lax.Precision.HIGHEST
    rank = basis.shape[1]
    buffer = momentum + gradient.astype(jnp.float32)
    panel_part = jnp.dot(buffer, basis, precision=highest)
    tensor_size = lax.axis_size("tensor")
    panel_full = scatter_gather_psum(panel_part, "tensor", tensor_size)
    gram_part = jnp.dot(panel_full.T, panel_full, precision=highest)
    block = 128
    fsdp_size = lax.axis_size("fsdp")
    gram_blocks = padded_scatter_gather_psum(lower_blocks(gram_part, block), "fsdp", fsdp_size)
    cross_part, gram_blocks = lax.optimization_barrier(
        (jnp.dot(buffer.T, panel_full, precision=highest), gram_blocks)
    )
    cross = padded_scatter_gather_psum(cross_part, "fsdp", fsdp_size)
    gram_matrix = symmetric_from_lower_blocks(gram_blocks, rank // block)
    factor = jnp.linalg.cholesky(gram_matrix)
    rows = panel_full.shape[0]
    inverse = lower_inverse(factor)
    solved = jnp.dot(jnp.concatenate([panel_full, cross], axis=0), inverse.T, precision=highest)
    orthonormal = solved[:rows]
    right_factor = solved[rows:]
    col_sumsq = gather_psum(jnp.sum(right_factor * right_factor, axis=0), "tensor", tensor_size)
    new_basis = right_factor / jnp.sqrt(col_sumsq + 1e-06)
    new_momentum = buffer - 0.1 * jnp.dot(orthonormal, right_factor.T, precision=highest)
    total_rows = buffer.shape[0] * lax.axis_size("fsdp")
    total_cols = buffer.shape[1] * lax.axis_size("tensor")
    step_scale = 0.2 * jnp.sqrt(jnp.float32(total_rows * total_cols / basis.shape[1]))
    update = jnp.dot(orthonormal, new_basis.T, precision=highest)
    new_weight = (weight.astype(jnp.float32) - step_scale * update).astype(jnp.bfloat16)
    return (new_momentum, new_basis, new_weight)


def solution(mesh):
    placed = (P("fsdp", "tensor"), P("fsdp", "tensor"), P("fsdp", "tensor"), P("tensor", None))
    return jax.shard_map(
        local,
        mesh=mesh,
        in_specs=placed,
        out_specs=(P("fsdp", "tensor"), P("tensor", None), P("fsdp", "tensor")),
        check_vma=False,
    )
```

```python
import jax
import jax.numpy as jnp
from jax import lax
from jax.sharding import PartitionSpec as P


def scatter_gather_psum(x, axis, size):
    chunks = x.reshape(size, -1, 128)
    mine = jnp.sum(lax.all_to_all(chunks, axis, 0, 0, tiled=False), axis=0)
    spread = jnp.broadcast_to(mine[None], chunks.shape)
    return lax.all_to_all(spread, axis, 0, 0, tiled=False).reshape(x.shape)


def padded_scatter_psum(x, axis, size):
    flat = x.reshape(-1)
    chunk = size * 8 * 128
    padded = jnp.pad(flat, (0, (-flat.shape[0]) % chunk))
    chunks = padded.reshape(size, -1, 128)
    return jnp.sum(lax.all_to_all(chunks, axis, 0, 0, tiled=False), axis=0)


def padded_gather(mine, axis, size, like):
    spread = jnp.broadcast_to(mine[None], (size,) + mine.shape)
    whole = lax.all_to_all(spread, axis, 0, 0, tiled=False).reshape(-1)
    return whole[: like.size].reshape(like.shape)


def lower_blocks(matrix, block):
    count = matrix.shape[0] // block
    return jnp.stack([matrix[i * block:(i + 1) * block, j * block:(j + 1) * block] for i in range(count) for j in range(i + 1)])


def symmetric_from_lower_blocks(blocks, count):
    block = blocks.shape[-1]
    index = {}
    for i in range(count):
        for j in range(i + 1):
            index[(i, j)] = len(index)
    rows = []
    for i in range(count):
        row = [blocks[index[(i, j)]] if j <= i else blocks[index[(j, i)]].T for j in range(count)]
        rows.append(jnp.concatenate(row, axis=1))
    return jnp.concatenate(rows, axis=0)


def lower_inverse(factor):
    size = factor.shape[0]
    levels = [factor[None]]
    while levels[-1].shape[-1] > 1:
        blocks = levels[-1]
        half = blocks.shape[-1] // 2
        pair = jnp.stack([blocks[:, :half, :half], blocks[:, half:, half:]], axis=1)
        levels.append(pair.reshape(-1, half, half))
    inverse = 1.0 / levels[-1]
    for blocks in reversed(levels[:-1]):
        width = blocks.shape[-1] // 2
        upper = inverse[0::2]
        lower = inverse[1::2]
        corner = blocks[:, width:, :width]
        off = -jnp.matmul(jnp.matmul(lower, corner, precision=lax.Precision.HIGHEST), upper, precision=lax.Precision.HIGHEST)
        top = jnp.concatenate([upper, jnp.zeros_like(upper)], axis=2)
        bottom = jnp.concatenate([off, lower], axis=2)
        inverse = jnp.concatenate([top, bottom], axis=1)
    return inverse[0]


def gather_psum(x, axis, size):
    copies = jnp.broadcast_to(x[None], (size,) + x.shape)
    return jnp.sum(lax.all_to_all(copies, axis, 0, 0, tiled=False), axis=0)


def local(momentum, gradient, weight, basis):
    highest = lax.Precision.HIGHEST
    rank = basis.shape[1]
    buffer = momentum + gradient.astype(jnp.float32)
    panel_part = jnp.dot(buffer, basis, precision=highest)
    tensor_size = lax.axis_size("tensor")
    panel_full = scatter_gather_psum(panel_part, "tensor", tensor_size)
    gram_part = jnp.dot(panel_full.T, panel_full, precision=highest)
    block = 128
    fsdp_size = lax.axis_size("fsdp")
    gram_lower = lower_blocks(gram_part, block)
    gram_mine = padded_scatter_psum(gram_lower, "fsdp", fsdp_size)
    cross_part, gram_mine = lax.optimization_barrier((jnp.dot(buffer.T, panel_full, precision=highest), gram_mine))
    gram_blocks = padded_gather(gram_mine, "fsdp", fsdp_size, gram_lower)
    cross_mine = padded_scatter_psum(cross_part, "fsdp", fsdp_size)
    gram_blocks, cross_mine = lax.optimization_barrier((gram_blocks, cross_mine))
    cross = padded_gather(cross_mine, "fsdp", fsdp_size, cross_part)
    gram_matrix = symmetric_from_lower_blocks(gram_blocks, rank // block)
    factor = jnp.linalg.cholesky(gram_matrix)
    factor, cross = lax.optimization_barrier((factor, cross))
    rows = panel_full.shape[0]
    inverse = lower_inverse(factor)
    solved = jnp.dot(jnp.concatenate([panel_full, cross], axis=0), inverse.T, precision=highest)
    orthonormal = solved[:rows]
    right_factor = solved[rows:]
    col_sumsq = gather_psum(jnp.sum(right_factor * right_factor, axis=0), "tensor", tensor_size)
    new_basis = right_factor / jnp.sqrt(col_sumsq + 1e-06)
    new_momentum = buffer - 0.1 * jnp.dot(orthonormal, right_factor.T, precision=highest)
    total_rows = buffer.shape[0] * lax.axis_size("fsdp")
    total_cols = buffer.shape[1] * lax.axis_size("tensor")
    step_scale = 0.2 * jnp.sqrt(jnp.float32(total_rows * total_cols / basis.shape[1]))
    update = jnp.dot(orthonormal, new_basis.T, precision=highest)
    new_weight = (weight.astype(jnp.float32) - step_scale * update).astype(jnp.bfloat16)
    return (new_momentum, new_basis, new_weight)


def solution(mesh):
    placed = (P("fsdp", "tensor"), P("fsdp", "tensor"), P("fsdp", "tensor"), P("tensor", None))
    return jax.shard_map(
        local,
        mesh=mesh,
        in_specs=placed,
        out_specs=(P("fsdp", "tensor"), P("tensor", None), P("fsdp", "tensor")),
        check_vma=False,
    )
```

```python
import jax
import jax.numpy as jnp
from jax import lax
from jax.sharding import PartitionSpec as P


def scatter_gather_psum(x, axis, size):
    chunks = x.reshape(size, -1, 128)
    mine = jnp.sum(lax.all_to_all(chunks, axis, 0, 0, tiled=False), axis=0)
    spread = jnp.broadcast_to(mine[None], chunks.shape)
    return lax.all_to_all(spread, axis, 0, 0, tiled=False).reshape(x.shape)


def padded_scatter_psum(x, axis, size):
    flat = x.reshape(-1)
    chunk = size * 8 * 128
    padded = jnp.pad(flat, (0, (-flat.shape[0]) % chunk))
    chunks = padded.reshape(size, -1, 128)
    return jnp.sum(lax.all_to_all(chunks, axis, 0, 0, tiled=False), axis=0)


def padded_gather(mine, axis, size, like):
    spread = jnp.broadcast_to(mine[None], (size,) + mine.shape)
    whole = lax.all_to_all(spread, axis, 0, 0, tiled=False).reshape(-1)
    return whole[: like.size].reshape(like.shape)


def lower_blocks(matrix, block):
    count = matrix.shape[0] // block
    return jnp.stack([matrix[i * block:(i + 1) * block, j * block:(j + 1) * block] for i in range(count) for j in range(i + 1)])


def symmetric_from_lower_blocks(blocks, count):
    block = blocks.shape[-1]
    index = {}
    for i in range(count):
        for j in range(i + 1):
            index[(i, j)] = len(index)
    rows = []
    for i in range(count):
        row = [blocks[index[(i, j)]] if j <= i else blocks[index[(j, i)]].T for j in range(count)]
        rows.append(jnp.concatenate(row, axis=1))
    return jnp.concatenate(rows, axis=0)


def lower_inverse(factor):
    size = factor.shape[0]
    levels = [factor[None]]
    while levels[-1].shape[-1] > 1:
        blocks = levels[-1]
        half = blocks.shape[-1] // 2
        pair = jnp.stack([blocks[:, :half, :half], blocks[:, half:, half:]], axis=1)
        levels.append(pair.reshape(-1, half, half))
    inverse = 1.0 / levels[-1]
    for blocks in reversed(levels[:-1]):
        width = blocks.shape[-1] // 2
        upper = inverse[0::2]
        lower = inverse[1::2]
        corner = blocks[:, width:, :width]
        off = -jnp.matmul(jnp.matmul(lower, corner, precision=lax.Precision.HIGHEST), upper, precision=lax.Precision.HIGHEST)
        top = jnp.concatenate([upper, jnp.zeros_like(upper)], axis=2)
        bottom = jnp.concatenate([off, lower], axis=2)
        inverse = jnp.concatenate([top, bottom], axis=1)
    return inverse[0]


def gather_psum(x, axis, size):
    copies = jnp.broadcast_to(x[None], (size,) + x.shape)
    return jnp.sum(lax.all_to_all(copies, axis, 0, 0, tiled=False), axis=0)


def local(momentum, gradient, weight, basis):
    highest = lax.Precision.HIGHEST
    rank = basis.shape[1]
    buffer = momentum + gradient.astype(jnp.float32)
    panel_part = jnp.dot(buffer, basis, precision=highest)
    tensor_size = lax.axis_size("tensor")
    panel_full = scatter_gather_psum(panel_part, "tensor", tensor_size)
    gram_part = jnp.dot(panel_full.T, panel_full, precision=highest)
    block = 128
    fsdp_size = lax.axis_size("fsdp")
    gram_lower = lower_blocks(gram_part, block)
    gram_blocks = padded_gather(padded_scatter_psum(gram_lower, "fsdp", fsdp_size), "fsdp", fsdp_size, gram_lower)
    cross_part, gram_blocks = lax.optimization_barrier((jnp.dot(buffer.T, panel_full, precision=highest), gram_blocks))
    cross_mine = padded_scatter_psum(cross_part, "fsdp", fsdp_size)
    gram_matrix = symmetric_from_lower_blocks(gram_blocks, rank // block)
    factor = jnp.linalg.cholesky(gram_matrix)
    factor, cross_mine = lax.optimization_barrier((factor, cross_mine))
    cross = padded_gather(cross_mine, "fsdp", fsdp_size, cross_part)
    rows = panel_full.shape[0]
    inverse = lower_inverse(factor)
    solved = jnp.dot(jnp.concatenate([panel_full, cross], axis=0), inverse.T, precision=highest)
    orthonormal = solved[:rows]
    right_factor = solved[rows:]
    col_sumsq = gather_psum(jnp.sum(right_factor * right_factor, axis=0), "tensor", tensor_size)
    new_basis = right_factor / jnp.sqrt(col_sumsq + 1e-06)
    new_momentum = buffer - 0.1 * jnp.dot(orthonormal, right_factor.T, precision=highest)
    total_rows = buffer.shape[0] * lax.axis_size("fsdp")
    total_cols = buffer.shape[1] * lax.axis_size("tensor")
    step_scale = 0.2 * jnp.sqrt(jnp.float32(total_rows * total_cols / basis.shape[1]))
    update = jnp.dot(orthonormal, new_basis.T, precision=highest)
    new_weight = (weight.astype(jnp.float32) - step_scale * update).astype(jnp.bfloat16)
    return (new_momentum, new_basis, new_weight)


def solution(mesh):
    placed = (P("fsdp", "tensor"), P("fsdp", "tensor"), P("fsdp", "tensor"), P("tensor", None))
    return jax.shard_map(
        local,
        mesh=mesh,
        in_specs=placed,
        out_specs=(P("fsdp", "tensor"), P("tensor", None), P("fsdp", "tensor")),
        check_vma=False,
    )
```

```python
import jax
import jax.numpy as jnp
from jax import lax
from jax.sharding import PartitionSpec as P


def scatter_gather_psum(x, axis, size):
    chunks = x.reshape(size, -1, 128)
    mine = jnp.sum(lax.all_to_all(chunks, axis, 0, 0, tiled=False), axis=0)
    spread = jnp.broadcast_to(mine[None], chunks.shape)
    return lax.all_to_all(spread, axis, 0, 0, tiled=False).reshape(x.shape)


def padded_scatter_psum(x, axis, size):
    flat = x.reshape(-1)
    chunk = size * 8 * 128
    padded = jnp.pad(flat, (0, (-flat.shape[0]) % chunk))
    chunks = padded.reshape(size, -1, 128)
    return jnp.sum(lax.all_to_all(chunks, axis, 0, 0, tiled=False), axis=0)


def padded_gather(mine, axis, size, like):
    spread = jnp.broadcast_to(mine[None], (size,) + mine.shape)
    whole = lax.all_to_all(spread, axis, 0, 0, tiled=False).reshape(-1)
    return whole[: like.size].reshape(like.shape)


def lower_blocks(matrix, block):
    count = matrix.shape[0] // block
    return jnp.stack([matrix[i * block:(i + 1) * block, j * block:(j + 1) * block] for i in range(count) for j in range(i + 1)])


def symmetric_from_lower_blocks(blocks, count):
    block = blocks.shape[-1]
    index = {}
    for i in range(count):
        for j in range(i + 1):
            index[(i, j)] = len(index)
    rows = []
    for i in range(count):
        row = [blocks[index[(i, j)]] if j <= i else blocks[index[(j, i)]].T for j in range(count)]
        rows.append(jnp.concatenate(row, axis=1))
    return jnp.concatenate(rows, axis=0)


def lower_inverse(factor):
    size = factor.shape[0]
    levels = [factor[None]]
    while levels[-1].shape[-1] > 1:
        blocks = levels[-1]
        half = blocks.shape[-1] // 2
        pair = jnp.stack([blocks[:, :half, :half], blocks[:, half:, half:]], axis=1)
        levels.append(pair.reshape(-1, half, half))
    inverse = 1.0 / levels[-1]
    for blocks in reversed(levels[:-1]):
        width = blocks.shape[-1] // 2
        upper = inverse[0::2]
        lower = inverse[1::2]
        corner = blocks[:, width:, :width]
        off = -jnp.matmul(jnp.matmul(lower, corner, precision=lax.Precision.HIGHEST), upper, precision=lax.Precision.HIGHEST)
        top = jnp.concatenate([upper, jnp.zeros_like(upper)], axis=2)
        bottom = jnp.concatenate([off, lower], axis=2)
        inverse = jnp.concatenate([top, bottom], axis=1)
    return inverse[0]


def gather_psum(x, axis, size):
    copies = jnp.broadcast_to(x[None], (size,) + x.shape)
    return jnp.sum(lax.all_to_all(copies, axis, 0, 0, tiled=False), axis=0)


def local(momentum, gradient, weight, basis):
    highest = lax.Precision.HIGHEST
    rank = basis.shape[1]
    buffer = momentum + gradient.astype(jnp.float32)
    panel_part = jnp.dot(buffer, basis, precision=highest)
    tensor_size = lax.axis_size("tensor")
    panel_full = scatter_gather_psum(panel_part, "tensor", tensor_size)
    gram_part = jnp.dot(panel_full.T, panel_full, precision=highest)
    block = 128
    fsdp_size = lax.axis_size("fsdp")
    gram_lower = lower_blocks(gram_part, block)
    gram_blocks = padded_gather(padded_scatter_psum(gram_lower, "fsdp", fsdp_size), "fsdp", fsdp_size, gram_lower)
    cross_part, gram_blocks = lax.optimization_barrier((jnp.dot(buffer.T, panel_full, precision=highest), gram_blocks))
    cross_mine = padded_scatter_psum(cross_part, "fsdp", fsdp_size)
    gram_matrix = symmetric_from_lower_blocks(gram_blocks, rank // block)
    cross = padded_gather(cross_mine, "fsdp", fsdp_size, cross_part)
    factor = jnp.linalg.cholesky(gram_matrix)
    factor, cross = lax.optimization_barrier((factor, cross))
    rows = panel_full.shape[0]
    inverse = lower_inverse(factor)
    solved = jnp.dot(jnp.concatenate([panel_full, cross], axis=0), inverse.T, precision=highest)
    orthonormal = solved[:rows]
    right_factor = solved[rows:]
    col_sumsq = gather_psum(jnp.sum(right_factor * right_factor, axis=0), "tensor", tensor_size)
    new_basis = right_factor / jnp.sqrt(col_sumsq + 1e-06)
    new_momentum = buffer - 0.1 * jnp.dot(orthonormal, right_factor.T, precision=highest)
    total_rows = buffer.shape[0] * lax.axis_size("fsdp")
    total_cols = buffer.shape[1] * lax.axis_size("tensor")
    step_scale = 0.2 * jnp.sqrt(jnp.float32(total_rows * total_cols / basis.shape[1]))
    update = jnp.dot(orthonormal, new_basis.T, precision=highest)
    new_weight = (weight.astype(jnp.float32) - step_scale * update).astype(jnp.bfloat16)
    return (new_momentum, new_basis, new_weight)


def solution(mesh):
    placed = (P("fsdp", "tensor"), P("fsdp", "tensor"), P("fsdp", "tensor"), P("tensor", None))
    return jax.shard_map(
        local,
        mesh=mesh,
        in_specs=placed,
        out_specs=(P("fsdp", "tensor"), P("tensor", None), P("fsdp", "tensor")),
        check_vma=False,
    )
```

```python
import jax
import jax.numpy as jnp
from jax import lax
from jax.sharding import PartitionSpec as P


def scatter_gather_psum(x, axis, size):
    chunks = x.reshape(size, -1, 128)
    mine = jnp.sum(lax.all_to_all(chunks, axis, 0, 0, tiled=False), axis=0)
    spread = jnp.broadcast_to(mine[None], chunks.shape)
    return lax.all_to_all(spread, axis, 0, 0, tiled=False).reshape(x.shape)


def padded_scatter_psum(x, axis, size):
    flat = x.reshape(-1)
    chunk = size * 8 * 128
    padded = jnp.pad(flat, (0, (-flat.shape[0]) % chunk))
    chunks = padded.reshape(size, -1, 128)
    return jnp.sum(lax.all_to_all(chunks, axis, 0, 0, tiled=False), axis=0)


def padded_gather(mine, axis, size, like):
    spread = jnp.broadcast_to(mine[None], (size,) + mine.shape)
    whole = lax.all_to_all(spread, axis, 0, 0, tiled=False).reshape(-1)
    return whole[: like.size].reshape(like.shape)


def lower_blocks(matrix, block):
    count = matrix.shape[0] // block
    return jnp.stack([matrix[i * block:(i + 1) * block, j * block:(j + 1) * block] for i in range(count) for j in range(i + 1)])


def symmetric_from_lower_blocks(blocks, count):
    block = blocks.shape[-1]
    index = {}
    for i in range(count):
        for j in range(i + 1):
            index[(i, j)] = len(index)
    rows = []
    for i in range(count):
        row = [blocks[index[(i, j)]] if j <= i else blocks[index[(j, i)]].T for j in range(count)]
        rows.append(jnp.concatenate(row, axis=1))
    return jnp.concatenate(rows, axis=0)


def lower_inverse(factor):
    size = factor.shape[0]
    levels = [factor[None]]
    while levels[-1].shape[-1] > 1:
        blocks = levels[-1]
        half = blocks.shape[-1] // 2
        pair = jnp.stack([blocks[:, :half, :half], blocks[:, half:, half:]], axis=1)
        levels.append(pair.reshape(-1, half, half))
    inverse = 1.0 / levels[-1]
    for blocks in reversed(levels[:-1]):
        width = blocks.shape[-1] // 2
        upper = inverse[0::2]
        lower = inverse[1::2]
        corner = blocks[:, width:, :width]
        off = -jnp.matmul(jnp.matmul(lower, corner, precision=lax.Precision.HIGHEST), upper, precision=lax.Precision.HIGHEST)
        top = jnp.concatenate([upper, jnp.zeros_like(upper)], axis=2)
        bottom = jnp.concatenate([off, lower], axis=2)
        inverse = jnp.concatenate([top, bottom], axis=1)
    return inverse[0]


def gather_psum(x, axis, size):
    copies = jnp.broadcast_to(x[None], (size,) + x.shape)
    return jnp.sum(lax.all_to_all(copies, axis, 0, 0, tiled=False), axis=0)


def local(momentum, gradient, weight, basis):
    highest = lax.Precision.HIGHEST
    rank = basis.shape[1]
    buffer = momentum + gradient.astype(jnp.float32)
    panel_part = jnp.dot(buffer, basis, precision=highest)
    tensor_size = lax.axis_size("tensor")
    panel_full = scatter_gather_psum(panel_part, "tensor", tensor_size)
    gram_part = jnp.dot(panel_full.T, panel_full, precision=highest)
    block = 64
    fsdp_size = lax.axis_size("fsdp")
    gram_lower = lower_blocks(gram_part, block)
    flat = gram_lower.reshape(-1)
    flat = jnp.pad(flat, (0, (-flat.shape[0]) % (tensor_size * 128)))
    share = lax.dynamic_index_in_dim(flat.reshape(tensor_size, -1, 128), lax.axis_index("tensor"), 0, keepdims=False)
    share = gather_psum(share, "fsdp", fsdp_size)
    shares = lax.all_to_all(jnp.broadcast_to(share[None], (tensor_size,) + share.shape), "tensor", 0, 0, tiled=False)
    gram_blocks = shares.reshape(-1)[: gram_lower.size].reshape(gram_lower.shape)
    cross_part, gram_blocks = lax.optimization_barrier((jnp.dot(buffer.T, panel_full, precision=highest), gram_blocks))
    cross_mine = padded_scatter_psum(cross_part, "fsdp", fsdp_size)
    gram_matrix = symmetric_from_lower_blocks(gram_blocks, rank // block)
    cross = padded_gather(cross_mine, "fsdp", fsdp_size, cross_part)
    factor = jnp.linalg.cholesky(gram_matrix)
    factor, cross = lax.optimization_barrier((factor, cross))
    rows = panel_full.shape[0]
    inverse = lower_inverse(factor)
    solved = jnp.dot(jnp.concatenate([panel_full, cross], axis=0), inverse.T, precision=highest)
    orthonormal = solved[:rows]
    right_factor = solved[rows:]
    col_sumsq = gather_psum(jnp.sum(right_factor * right_factor, axis=0), "tensor", tensor_size)
    new_basis = right_factor / jnp.sqrt(col_sumsq + 1e-06)
    new_momentum = buffer - 0.1 * jnp.dot(orthonormal, right_factor.T, precision=highest)
    total_rows = buffer.shape[0] * lax.axis_size("fsdp")
    total_cols = buffer.shape[1] * lax.axis_size("tensor")
    step_scale = 0.2 * jnp.sqrt(jnp.float32(total_rows * total_cols / basis.shape[1]))
    update = jnp.dot(orthonormal, new_basis.T, precision=highest)
    new_weight = (weight.astype(jnp.float32) - step_scale * update).astype(jnp.bfloat16)
    return (new_momentum, new_basis, new_weight)


def solution(mesh):
    placed = (P("fsdp", "tensor"), P("fsdp", "tensor"), P("fsdp", "tensor"), P("tensor", None))
    return jax.shard_map(
        local,
        mesh=mesh,
        in_specs=placed,
        out_specs=(P("fsdp", "tensor"), P("tensor", None), P("fsdp", "tensor")),
        check_vma=False,
    )
```

```python
import jax
import jax.numpy as jnp
from jax import lax
from jax.sharding import PartitionSpec as P


def scatter_gather_psum(x, axis, size):
    chunks = x.reshape(size, -1, 128)
    mine = jnp.sum(lax.all_to_all(chunks, axis, 0, 0, tiled=False), axis=0)
    spread = jnp.broadcast_to(mine[None], chunks.shape)
    return lax.all_to_all(spread, axis, 0, 0, tiled=False).reshape(x.shape)


def padded_scatter_psum(x, axis, size):
    flat = x.reshape(-1)
    chunk = size * 8 * 128
    padded = jnp.pad(flat, (0, (-flat.shape[0]) % chunk))
    chunks = padded.reshape(size, -1, 128)
    return jnp.sum(lax.all_to_all(chunks, axis, 0, 0, tiled=False), axis=0)


def padded_gather(mine, axis, size, like):
    spread = jnp.broadcast_to(mine[None], (size,) + mine.shape)
    whole = lax.all_to_all(spread, axis, 0, 0, tiled=False).reshape(-1)
    return whole[: like.size].reshape(like.shape)


def lower_blocks(matrix, block):
    count = matrix.shape[0] // block
    return jnp.stack([matrix[i * block:(i + 1) * block, j * block:(j + 1) * block] for i in range(count) for j in range(i + 1)])


def symmetric_from_lower_blocks(blocks, count):
    block = blocks.shape[-1]
    index = {}
    for i in range(count):
        for j in range(i + 1):
            index[(i, j)] = len(index)
    rows = []
    for i in range(count):
        row = [blocks[index[(i, j)]] if j <= i else blocks[index[(j, i)]].T for j in range(count)]
        rows.append(jnp.concatenate(row, axis=1))
    return jnp.concatenate(rows, axis=0)


def lower_inverse(factor):
    size = factor.shape[0]
    levels = [factor[None]]
    while levels[-1].shape[-1] > 1:
        blocks = levels[-1]
        half = blocks.shape[-1] // 2
        pair = jnp.stack([blocks[:, :half, :half], blocks[:, half:, half:]], axis=1)
        levels.append(pair.reshape(-1, half, half))
    inverse = 1.0 / levels[-1]
    for blocks in reversed(levels[:-1]):
        width = blocks.shape[-1] // 2
        upper = inverse[0::2]
        lower = inverse[1::2]
        corner = blocks[:, width:, :width]
        off = -jnp.matmul(jnp.matmul(lower, corner, precision=lax.Precision.HIGHEST), upper, precision=lax.Precision.HIGHEST)
        top = jnp.concatenate([upper, jnp.zeros_like(upper)], axis=2)
        bottom = jnp.concatenate([off, lower], axis=2)
        inverse = jnp.concatenate([top, bottom], axis=1)
    return inverse[0]


def gather_psum(x, axis, size):
    copies = jnp.broadcast_to(x[None], (size,) + x.shape)
    return jnp.sum(lax.all_to_all(copies, axis, 0, 0, tiled=False), axis=0)


def local(momentum, gradient, weight, basis):
    highest = lax.Precision.HIGHEST
    rank = basis.shape[1]
    buffer = momentum + gradient.astype(jnp.float32)
    panel_part = jnp.dot(buffer, basis, precision=highest)
    tensor_size = lax.axis_size("tensor")
    panel_full = scatter_gather_psum(panel_part, "tensor", tensor_size)
    gram_part = jnp.dot(panel_full.T, panel_full, precision=highest)
    block = 128
    fsdp_size = lax.axis_size("fsdp")
    gram_lower = lower_blocks(gram_part, block)
    flat = gram_lower.reshape(-1)
    flat = jnp.pad(flat, (0, (-flat.shape[0]) % (tensor_size * 128)))
    share = lax.dynamic_index_in_dim(flat.reshape(tensor_size, -1, 128), lax.axis_index("tensor"), 0, keepdims=False)
    share = gather_psum(share, "fsdp", fsdp_size)
    shares = lax.all_to_all(jnp.broadcast_to(share[None], (tensor_size,) + share.shape), "tensor", 0, 0, tiled=False)
    gram_blocks = shares.reshape(-1)[: gram_lower.size].reshape(gram_lower.shape)
    cross_part, gram_blocks = lax.optimization_barrier((jnp.dot(buffer.T, panel_full, precision=highest), gram_blocks))
    cross_mine = padded_scatter_psum(cross_part, "fsdp", fsdp_size)
    gram_matrix = symmetric_from_lower_blocks(gram_blocks, rank // block)
    cross = padded_gather(cross_mine, "fsdp", fsdp_size, cross_part)
    factor = jnp.linalg.cholesky(gram_matrix)
    factor, cross = lax.optimization_barrier((factor, cross))
    rows = panel_full.shape[0]
    inverse = lower_inverse(factor)
    solved = jnp.dot(jnp.concatenate([panel_full, cross], axis=0), inverse.T, precision=highest)
    orthonormal = solved[:rows]
    right_factor = solved[rows:]
    col_sumsq = gather_psum(jnp.sum(right_factor * right_factor, axis=0), "tensor", tensor_size)
    new_basis = right_factor / jnp.sqrt(col_sumsq + 1e-06)
    new_momentum = buffer - 0.1 * jnp.dot(orthonormal, right_factor.T, precision=highest)
    total_rows = buffer.shape[0] * lax.axis_size("fsdp")
    total_cols = buffer.shape[1] * lax.axis_size("tensor")
    step_scale = 0.2 * jnp.sqrt(jnp.float32(total_rows * total_cols / basis.shape[1]))
    update = jnp.dot(orthonormal, new_basis.T, precision=highest)
    new_weight = (weight.astype(jnp.float32) - step_scale * update).astype(jnp.bfloat16)
    return (new_momentum, new_basis, new_weight)


def solution(mesh):
    placed = (P("fsdp", "tensor"), P("fsdp", "tensor"), P("fsdp", "tensor"), P("tensor", None))
    return jax.shard_map(
        local,
        mesh=mesh,
        in_specs=placed,
        out_specs=(P("fsdp", "tensor"), P("tensor", None), P("fsdp", "tensor")),
        check_vma=False,
    )
```

```python
import jax
import jax.numpy as jnp
from jax import lax
from jax.sharding import PartitionSpec as P


def scatter_gather_psum(x, axis, size):
    chunks = x.reshape(size, -1, 128)
    mine = jnp.sum(lax.all_to_all(chunks, axis, 0, 0, tiled=False), axis=0)
    spread = jnp.broadcast_to(mine[None], chunks.shape)
    return lax.all_to_all(spread, axis, 0, 0, tiled=False).reshape(x.shape)


def padded_scatter_psum(x, axis, size):
    flat = x.reshape(-1)
    chunk = size * 8 * 128
    padded = jnp.pad(flat, (0, (-flat.shape[0]) % chunk))
    chunks = padded.reshape(size, -1, 128)
    return jnp.sum(lax.all_to_all(chunks, axis, 0, 0, tiled=False), axis=0)


def padded_gather(mine, axis, size, like):
    spread = jnp.broadcast_to(mine[None], (size,) + mine.shape)
    whole = lax.all_to_all(spread, axis, 0, 0, tiled=False).reshape(-1)
    return whole[: like.size].reshape(like.shape)


def lower_blocks(matrix, block):
    count = matrix.shape[0] // block
    return jnp.stack([matrix[i * block:(i + 1) * block, j * block:(j + 1) * block] for i in range(count) for j in range(i + 1)])


def symmetric_from_lower_blocks(blocks, count):
    block = blocks.shape[-1]
    index = {}
    for i in range(count):
        for j in range(i + 1):
            index[(i, j)] = len(index)
    rows = []
    for i in range(count):
        row = [blocks[index[(i, j)]] if j <= i else blocks[index[(j, i)]].T for j in range(count)]
        rows.append(jnp.concatenate(row, axis=1))
    return jnp.concatenate(rows, axis=0)


def lower_inverse(factor):
    leaf = 8
    levels = [factor[None]]
    while levels[-1].shape[-1] > leaf:
        blocks = levels[-1]
        half = blocks.shape[-1] // 2
        pair = jnp.stack([blocks[:, :half, :half], blocks[:, half:, half:]], axis=1)
        levels.append(pair.reshape(-1, half, half))
    unit = jnp.eye(leaf, dtype=factor.dtype)
    diagonal = jnp.sum(levels[-1] * unit, axis=2)
    strict = levels[-1] / diagonal[:, :, None] - unit
    square = jnp.matmul(strict, strict, precision=lax.Precision.HIGHEST)
    fourth = jnp.matmul(square, square, precision=lax.Precision.HIGHEST)
    inverse = jnp.matmul(jnp.matmul(unit - strict, unit + square, precision=lax.Precision.HIGHEST), unit + fourth, precision=lax.Precision.HIGHEST)
    inverse = inverse / diagonal[:, None, :]
    for blocks in reversed(levels[:-1]):
        width = blocks.shape[-1] // 2
        upper = inverse[0::2]
        lower = inverse[1::2]
        corner = blocks[:, width:, :width]
        off = -jnp.matmul(jnp.matmul(lower, corner, precision=lax.Precision.HIGHEST), upper, precision=lax.Precision.HIGHEST)
        top = jnp.concatenate([upper, jnp.zeros_like(upper)], axis=2)
        bottom = jnp.concatenate([off, lower], axis=2)
        inverse = jnp.concatenate([top, bottom], axis=1)
    return inverse[0]


def gather_psum(x, axis, size):
    copies = jnp.broadcast_to(x[None], (size,) + x.shape)
    return jnp.sum(lax.all_to_all(copies, axis, 0, 0, tiled=False), axis=0)


def local(momentum, gradient, weight, basis):
    highest = lax.Precision.HIGHEST
    rank = basis.shape[1]
    buffer = momentum + gradient.astype(jnp.float32)
    panel_part = jnp.dot(buffer, basis, precision=highest)
    tensor_size = lax.axis_size("tensor")
    panel_full = scatter_gather_psum(panel_part, "tensor", tensor_size)
    gram_part = jnp.dot(panel_full.T, panel_full, precision=highest)
    block = 128
    fsdp_size = lax.axis_size("fsdp")
    gram_lower = lower_blocks(gram_part, block)
    flat = gram_lower.reshape(-1)
    flat = jnp.pad(flat, (0, (-flat.shape[0]) % (tensor_size * 128)))
    share = lax.dynamic_index_in_dim(flat.reshape(tensor_size, -1, 128), lax.axis_index("tensor"), 0, keepdims=False)
    share = gather_psum(share, "fsdp", fsdp_size)
    shares = lax.all_to_all(jnp.broadcast_to(share[None], (tensor_size,) + share.shape), "tensor", 0, 0, tiled=False)
    gram_blocks = shares.reshape(-1)[: gram_lower.size].reshape(gram_lower.shape)
    cross_part, gram_blocks = lax.optimization_barrier((jnp.dot(buffer.T, panel_full, precision=highest), gram_blocks))
    cross_mine = padded_scatter_psum(cross_part, "fsdp", fsdp_size)
    gram_matrix = symmetric_from_lower_blocks(gram_blocks, rank // block)
    cross = padded_gather(cross_mine, "fsdp", fsdp_size, cross_part)
    factor = jnp.linalg.cholesky(gram_matrix)
    factor, cross = lax.optimization_barrier((factor, cross))
    rows = panel_full.shape[0]
    inverse = lower_inverse(factor)
    solved = jnp.dot(jnp.concatenate([panel_full, cross], axis=0), inverse.T, precision=highest)
    orthonormal = solved[:rows]
    right_factor = solved[rows:]
    col_sumsq = gather_psum(jnp.sum(right_factor * right_factor, axis=0), "tensor", tensor_size)
    new_basis = right_factor / jnp.sqrt(col_sumsq + 1e-06)
    new_momentum = buffer - 0.1 * jnp.dot(orthonormal, right_factor.T, precision=highest)
    total_rows = buffer.shape[0] * lax.axis_size("fsdp")
    total_cols = buffer.shape[1] * lax.axis_size("tensor")
    step_scale = 0.2 * jnp.sqrt(jnp.float32(total_rows * total_cols / basis.shape[1]))
    update = jnp.dot(orthonormal, new_basis.T, precision=highest)
    new_weight = (weight.astype(jnp.float32) - step_scale * update).astype(jnp.bfloat16)
    return (new_momentum, new_basis, new_weight)


def solution(mesh):
    placed = (P("fsdp", "tensor"), P("fsdp", "tensor"), P("fsdp", "tensor"), P("tensor", None))
    return jax.shard_map(
        local,
        mesh=mesh,
        in_specs=placed,
        out_specs=(P("fsdp", "tensor"), P("tensor", None), P("fsdp", "tensor")),
        check_vma=False,
    )
```

```python
import jax
import jax.numpy as jnp
from jax import lax
from jax.sharding import PartitionSpec as P


def scatter_gather_psum(x, axis, size):
    chunks = x.reshape(size, -1, 128)
    mine = jnp.sum(lax.all_to_all(chunks, axis, 0, 0, tiled=False), axis=0)
    spread = jnp.broadcast_to(mine[None], chunks.shape)
    return lax.all_to_all(spread, axis, 0, 0, tiled=False).reshape(x.shape)


def padded_scatter_psum(x, axis, size):
    flat = x.reshape(-1)
    chunk = size * 8 * 128
    padded = jnp.pad(flat, (0, (-flat.shape[0]) % chunk))
    chunks = padded.reshape(size, -1, 128)
    return jnp.sum(lax.all_to_all(chunks, axis, 0, 0, tiled=False), axis=0)


def padded_gather(mine, axis, size, like):
    spread = jnp.broadcast_to(mine[None], (size,) + mine.shape)
    whole = lax.all_to_all(spread, axis, 0, 0, tiled=False).reshape(-1)
    return whole[: like.size].reshape(like.shape)


def lower_blocks(matrix, block):
    count = matrix.shape[0] // block
    return jnp.stack([matrix[i * block:(i + 1) * block, j * block:(j + 1) * block] for i in range(count) for j in range(i + 1)])


def symmetric_from_lower_blocks(blocks, count):
    block = blocks.shape[-1]
    index = {}
    for i in range(count):
        for j in range(i + 1):
            index[(i, j)] = len(index)
    rows = []
    for i in range(count):
        row = [blocks[index[(i, j)]] if j <= i else blocks[index[(j, i)]].T for j in range(count)]
        rows.append(jnp.concatenate(row, axis=1))
    return jnp.concatenate(rows, axis=0)


def lower_inverse(factor):
    leaf = 8
    levels = [factor[None]]
    while levels[-1].shape[-1] > leaf:
        blocks = levels[-1]
        half = blocks.shape[-1] // 2
        pair = jnp.stack([blocks[:, :half, :half], blocks[:, half:, half:]], axis=1)
        levels.append(pair.reshape(-1, half, half))
    unit = jnp.eye(leaf, dtype=factor.dtype)
    diagonal = jnp.sum(levels[-1] * unit, axis=2)
    strict = levels[-1] / diagonal[:, :, None] - unit
    square = jnp.matmul(strict, strict, precision=lax.Precision.HIGHEST)
    fourth = jnp.matmul(square, square, precision=lax.Precision.HIGHEST)
    inverse = jnp.matmul(jnp.matmul(unit - strict, unit + square, precision=lax.Precision.HIGHEST), unit + fourth, precision=lax.Precision.HIGHEST)
    inverse = inverse / diagonal[:, None, :]
    for blocks in reversed(levels[:-1]):
        width = blocks.shape[-1] // 2
        upper = inverse[0::2]
        lower = inverse[1::2]
        corner = blocks[:, width:, :width]
        off = -jnp.matmul(jnp.matmul(lower, corner, precision=lax.Precision.HIGHEST), upper, precision=lax.Precision.HIGHEST)
        top = jnp.concatenate([upper, jnp.zeros_like(upper)], axis=2)
        bottom = jnp.concatenate([off, lower], axis=2)
        inverse = jnp.concatenate([top, bottom], axis=1)
    return inverse[0]


def blocked_cholesky(matrix, block, held, then):
    count = matrix.shape[0] // block
    rest = (matrix + matrix.T) * 0.5
    columns = []
    for k in range(count):
        if k == 1:
            rest, held = lax.optimization_barrier((rest, held))
            held = then(held)
        if k == count - 1:
            rest, held = lax.optimization_barrier((rest, held))
        head = jnp.linalg.cholesky(rest[:block, :block])
        below = rest[block:, :block]
        if k + 1 < count:
            panel = jnp.dot(below, lower_inverse(head).T, precision=lax.Precision.HIGHEST)
            rest = rest[block:, block:] - jnp.dot(panel, panel.T, precision=lax.Precision.HIGHEST)
            columns.append(jnp.concatenate([head, panel], axis=0))
        else:
            columns.append(head)
    size = matrix.shape[0]
    factor = jnp.concatenate([jnp.pad(c, ((size - c.shape[0], 0), (0, 0))) for c in columns], axis=1)
    return factor, held


def gather_psum(x, axis, size):
    copies = jnp.broadcast_to(x[None], (size,) + x.shape)
    return jnp.sum(lax.all_to_all(copies, axis, 0, 0, tiled=False), axis=0)


def local(momentum, gradient, weight, basis):
    highest = lax.Precision.HIGHEST
    rank = basis.shape[1]
    buffer = momentum + gradient.astype(jnp.float32)
    panel_part = jnp.dot(buffer, basis, precision=highest)
    tensor_size = lax.axis_size("tensor")
    panel_full = scatter_gather_psum(panel_part, "tensor", tensor_size)
    gram_part = jnp.dot(panel_full.T, panel_full, precision=highest)
    block = 128
    fsdp_size = lax.axis_size("fsdp")
    gram_lower = lower_blocks(gram_part, block)
    flat = gram_lower.reshape(-1)
    flat = jnp.pad(flat, (0, (-flat.shape[0]) % (tensor_size * 128)))
    share = lax.dynamic_index_in_dim(flat.reshape(tensor_size, -1, 128), lax.axis_index("tensor"), 0, keepdims=False)
    share = gather_psum(share, "fsdp", fsdp_size)
    shares = lax.all_to_all(jnp.broadcast_to(share[None], (tensor_size,) + share.shape), "tensor", 0, 0, tiled=False)
    gram_blocks = shares.reshape(-1)[: gram_lower.size].reshape(gram_lower.shape)
    cross_part, gram_blocks = lax.optimization_barrier((jnp.dot(buffer.T, panel_full, precision=highest), gram_blocks))
    cross_mine = padded_scatter_psum(cross_part, "fsdp", fsdp_size)
    gram_matrix = symmetric_from_lower_blocks(gram_blocks, rank // block)
    factor, cross = blocked_cholesky(
        gram_matrix, 128, cross_mine, lambda mine: padded_gather(mine, "fsdp", fsdp_size, cross_part)
    )
    factor, cross = lax.optimization_barrier((factor, cross))
    rows = panel_full.shape[0]
    inverse = lower_inverse(factor)
    solved = jnp.dot(jnp.concatenate([panel_full, cross], axis=0), inverse.T, precision=highest)
    orthonormal = solved[:rows]
    right_factor = solved[rows:]
    col_sumsq = gather_psum(jnp.sum(right_factor * right_factor, axis=0), "tensor", tensor_size)
    new_basis = right_factor / jnp.sqrt(col_sumsq + 1e-06)
    new_momentum = buffer - 0.1 * jnp.dot(orthonormal, right_factor.T, precision=highest)
    total_rows = buffer.shape[0] * lax.axis_size("fsdp")
    total_cols = buffer.shape[1] * lax.axis_size("tensor")
    step_scale = 0.2 * jnp.sqrt(jnp.float32(total_rows * total_cols / basis.shape[1]))
    update = jnp.dot(orthonormal, new_basis.T, precision=highest)
    new_weight = (weight.astype(jnp.float32) - step_scale * update).astype(jnp.bfloat16)
    return (new_momentum, new_basis, new_weight)


def solution(mesh):
    placed = (P("fsdp", "tensor"), P("fsdp", "tensor"), P("fsdp", "tensor"), P("tensor", None))
    return jax.shard_map(
        local,
        mesh=mesh,
        in_specs=placed,
        out_specs=(P("fsdp", "tensor"), P("tensor", None), P("fsdp", "tensor")),
        check_vma=False,
    )
```

```python
import jax
import jax.numpy as jnp
from jax import lax
from jax.sharding import PartitionSpec as P


def scatter_gather_psum(x, axis, size):
    chunks = x.reshape(size, -1, 128)
    mine = jnp.sum(lax.all_to_all(chunks, axis, 0, 0, tiled=False), axis=0)
    spread = jnp.broadcast_to(mine[None], chunks.shape)
    return lax.all_to_all(spread, axis, 0, 0, tiled=False).reshape(x.shape)


def padded_scatter_psum(x, axis, size):
    flat = x.reshape(-1)
    chunk = size * 8 * 128
    padded = jnp.pad(flat, (0, (-flat.shape[0]) % chunk))
    chunks = padded.reshape(size, -1, 128)
    return jnp.sum(lax.all_to_all(chunks, axis, 0, 0, tiled=False), axis=0)


def padded_gather(mine, axis, size, like):
    spread = jnp.broadcast_to(mine[None], (size,) + mine.shape)
    whole = lax.all_to_all(spread, axis, 0, 0, tiled=False).reshape(-1)
    return whole[: like.size].reshape(like.shape)


def lower_blocks(matrix, block):
    count = matrix.shape[0] // block
    return jnp.stack([matrix[i * block:(i + 1) * block, j * block:(j + 1) * block] for i in range(count) for j in range(i + 1)])


def symmetric_from_lower_blocks(blocks, count):
    block = blocks.shape[-1]
    index = {}
    for i in range(count):
        for j in range(i + 1):
            index[(i, j)] = len(index)
    rows = []
    for i in range(count):
        row = [blocks[index[(i, j)]] if j <= i else blocks[index[(j, i)]].T for j in range(count)]
        rows.append(jnp.concatenate(row, axis=1))
    return jnp.concatenate(rows, axis=0)


def lower_inverse(factor):
    leaf = 8
    levels = [factor[None]]
    while levels[-1].shape[-1] > leaf:
        blocks = levels[-1]
        half = blocks.shape[-1] // 2
        pair = jnp.stack([blocks[:, :half, :half], blocks[:, half:, half:]], axis=1)
        levels.append(pair.reshape(-1, half, half))
    unit = jnp.eye(leaf, dtype=factor.dtype)
    diagonal = jnp.sum(levels[-1] * unit, axis=2)
    strict = levels[-1] / diagonal[:, :, None] - unit
    square = jnp.matmul(strict, strict, precision=lax.Precision.HIGHEST)
    fourth = jnp.matmul(square, square, precision=lax.Precision.HIGHEST)
    inverse = jnp.matmul(jnp.matmul(unit - strict, unit + square, precision=lax.Precision.HIGHEST), unit + fourth, precision=lax.Precision.HIGHEST)
    inverse = inverse / diagonal[:, None, :]
    for blocks in reversed(levels[:-1]):
        width = blocks.shape[-1] // 2
        upper = inverse[0::2]
        lower = inverse[1::2]
        corner = blocks[:, width:, :width]
        off = -jnp.matmul(jnp.matmul(lower, corner, precision=lax.Precision.HIGHEST), upper, precision=lax.Precision.HIGHEST)
        top = jnp.concatenate([upper, jnp.zeros_like(upper)], axis=2)
        bottom = jnp.concatenate([off, lower], axis=2)
        inverse = jnp.concatenate([top, bottom], axis=1)
    return inverse[0]


def twelve_psum(x, axis):
    size = 12
    x = x + lax.ppermute(x, axis, [(i, i ^ 1) for i in range(size)])
    x = x + lax.ppermute(x, axis, [(i, i ^ 2) for i in range(size)])
    before = lax.ppermute(x, axis, [(i, (i + 4) % size) for i in range(size)])
    after = lax.ppermute(x, axis, [(i, (i - 4) % size) for i in range(size)])
    quad = lax.axis_index(axis) // 4
    first = jnp.where(quad == 0, x, jnp.where(quad == 1, before, after))
    second = jnp.where(quad == 0, after, jnp.where(quad == 1, x, before))
    third = jnp.where(quad == 0, before, jnp.where(quad == 1, after, x))
    return (first + second) + third


def gather_psum(x, axis, size):
    copies = jnp.broadcast_to(x[None], (size,) + x.shape)
    return jnp.sum(lax.all_to_all(copies, axis, 0, 0, tiled=False), axis=0)


def local(momentum, gradient, weight, basis):
    highest = lax.Precision.HIGHEST
    rank = basis.shape[1]
    buffer = momentum + gradient.astype(jnp.float32)
    panel_part = jnp.dot(buffer, basis, precision=highest)
    tensor_size = lax.axis_size("tensor")
    panel_full = scatter_gather_psum(panel_part, "tensor", tensor_size)
    gram_part = jnp.dot(panel_full.T, panel_full, precision=highest)
    block = 128
    fsdp_size = lax.axis_size("fsdp")
    gram_lower = lower_blocks(gram_part, block)
    flat = gram_lower.reshape(-1)
    flat = jnp.pad(flat, (0, (-flat.shape[0]) % (tensor_size * 128)))
    share = lax.dynamic_index_in_dim(flat.reshape(tensor_size, -1, 128), lax.axis_index("tensor"), 0, keepdims=False)
    share = twelve_psum(share, "fsdp") if fsdp_size == 12 else gather_psum(share, "fsdp", fsdp_size)
    shares = lax.all_to_all(jnp.broadcast_to(share[None], (tensor_size,) + share.shape), "tensor", 0, 0, tiled=False)
    gram_blocks = shares.reshape(-1)[: gram_lower.size].reshape(gram_lower.shape)
    cross_part, gram_blocks = lax.optimization_barrier((jnp.dot(buffer.T, panel_full, precision=highest), gram_blocks))
    cross_mine = padded_scatter_psum(cross_part, "fsdp", fsdp_size)
    gram_matrix = symmetric_from_lower_blocks(gram_blocks, rank // block)
    cross = padded_gather(cross_mine, "fsdp", fsdp_size, cross_part)
    factor = jnp.linalg.cholesky(gram_matrix)
    factor, cross = lax.optimization_barrier((factor, cross))
    rows = panel_full.shape[0]
    inverse = lower_inverse(factor)
    solved = jnp.dot(jnp.concatenate([panel_full, cross], axis=0), inverse.T, precision=highest)
    orthonormal = solved[:rows]
    right_factor = solved[rows:]
    col_sumsq = gather_psum(jnp.sum(right_factor * right_factor, axis=0), "tensor", tensor_size)
    new_basis = right_factor / jnp.sqrt(col_sumsq + 1e-06)
    new_momentum = buffer - 0.1 * jnp.dot(orthonormal, right_factor.T, precision=highest)
    total_rows = buffer.shape[0] * lax.axis_size("fsdp")
    total_cols = buffer.shape[1] * lax.axis_size("tensor")
    step_scale = 0.2 * jnp.sqrt(jnp.float32(total_rows * total_cols / basis.shape[1]))
    update = jnp.dot(orthonormal, new_basis.T, precision=highest)
    new_weight = (weight.astype(jnp.float32) - step_scale * update).astype(jnp.bfloat16)
    return (new_momentum, new_basis, new_weight)


def solution(mesh):
    placed = (P("fsdp", "tensor"), P("fsdp", "tensor"), P("fsdp", "tensor"), P("tensor", None))
    return jax.shard_map(
        local,
        mesh=mesh,
        in_specs=placed,
        out_specs=(P("fsdp", "tensor"), P("tensor", None), P("fsdp", "tensor")),
        check_vma=False,
    )
```

```python
import jax
import jax.numpy as jnp
from jax import lax
from jax.sharding import PartitionSpec as P


def scatter_gather_psum(x, axis, size):
    chunks = x.reshape(size, -1, 128)
    mine = jnp.sum(lax.all_to_all(chunks, axis, 0, 0, tiled=False), axis=0)
    spread = jnp.broadcast_to(mine[None], chunks.shape)
    return lax.all_to_all(spread, axis, 0, 0, tiled=False).reshape(x.shape)


def padded_scatter_psum(x, axis, size):
    flat = x.reshape(-1)
    chunk = size * 8 * 128
    padded = jnp.pad(flat, (0, (-flat.shape[0]) % chunk))
    chunks = padded.reshape(size, -1, 128)
    return jnp.sum(lax.all_to_all(chunks, axis, 0, 0, tiled=False), axis=0)


def padded_gather(mine, axis, size, like):
    spread = jnp.broadcast_to(mine[None], (size,) + mine.shape)
    whole = lax.all_to_all(spread, axis, 0, 0, tiled=False).reshape(-1)
    return whole[: like.size].reshape(like.shape)


def lower_blocks(matrix, block):
    count = matrix.shape[0] // block
    return jnp.stack([matrix[i * block:(i + 1) * block, j * block:(j + 1) * block] for i in range(count) for j in range(i + 1)])


def symmetric_from_lower_blocks(blocks, count):
    block = blocks.shape[-1]
    index = {}
    for i in range(count):
        for j in range(i + 1):
            index[(i, j)] = len(index)
    rows = []
    for i in range(count):
        row = [blocks[index[(i, j)]] if j <= i else blocks[index[(j, i)]].T for j in range(count)]
        rows.append(jnp.concatenate(row, axis=1))
    return jnp.concatenate(rows, axis=0)


def lower_inverse(factor):
    leaf = 16
    levels = [factor[None]]
    while levels[-1].shape[-1] > leaf:
        blocks = levels[-1]
        half = blocks.shape[-1] // 2
        pair = jnp.stack([blocks[:, :half, :half], blocks[:, half:, half:]], axis=1)
        levels.append(pair.reshape(-1, half, half))
    unit = jnp.eye(leaf, dtype=factor.dtype)
    diagonal = jnp.sum(levels[-1] * unit, axis=2)
    strict = levels[-1] / diagonal[:, :, None] - unit
    inverse = unit - strict
    power = strict
    span = 2
    while span < leaf:
        power = jnp.matmul(power, power, precision=lax.Precision.HIGHEST)
        inverse = jnp.matmul(inverse, unit + power, precision=lax.Precision.HIGHEST)
        span *= 2
    inverse = inverse / diagonal[:, None, :]
    for blocks in reversed(levels[:-1]):
        width = blocks.shape[-1] // 2
        upper = inverse[0::2]
        lower = inverse[1::2]
        corner = blocks[:, width:, :width]
        off = -jnp.matmul(jnp.matmul(lower, corner, precision=lax.Precision.HIGHEST), upper, precision=lax.Precision.HIGHEST)
        top = jnp.concatenate([upper, jnp.zeros_like(upper)], axis=2)
        bottom = jnp.concatenate([off, lower], axis=2)
        inverse = jnp.concatenate([top, bottom], axis=1)
    return inverse[0]


def gather_psum(x, axis, size):
    copies = jnp.broadcast_to(x[None], (size,) + x.shape)
    return jnp.sum(lax.all_to_all(copies, axis, 0, 0, tiled=False), axis=0)


def local(momentum, gradient, weight, basis):
    highest = lax.Precision.HIGHEST
    rank = basis.shape[1]
    buffer = momentum + gradient.astype(jnp.float32)
    panel_part = jnp.dot(buffer, basis, precision=highest)
    tensor_size = lax.axis_size("tensor")
    panel_full = scatter_gather_psum(panel_part, "tensor", tensor_size)
    gram_part = jnp.dot(panel_full.T, panel_full, precision=highest)
    block = 128
    fsdp_size = lax.axis_size("fsdp")
    gram_lower = lower_blocks(gram_part, block)
    flat = gram_lower.reshape(-1)
    flat = jnp.pad(flat, (0, (-flat.shape[0]) % (tensor_size * 128)))
    share = lax.dynamic_index_in_dim(flat.reshape(tensor_size, -1, 128), lax.axis_index("tensor"), 0, keepdims=False)
    share = gather_psum(share, "fsdp", fsdp_size)
    shares = lax.all_to_all(jnp.broadcast_to(share[None], (tensor_size,) + share.shape), "tensor", 0, 0, tiled=False)
    gram_blocks = shares.reshape(-1)[: gram_lower.size].reshape(gram_lower.shape)
    cross_part, gram_blocks = lax.optimization_barrier((jnp.dot(buffer.T, panel_full, precision=highest), gram_blocks))
    cross_mine = padded_scatter_psum(cross_part, "fsdp", fsdp_size)
    gram_matrix = symmetric_from_lower_blocks(gram_blocks, rank // block)
    cross = padded_gather(cross_mine, "fsdp", fsdp_size, cross_part)
    factor = jnp.linalg.cholesky(gram_matrix)
    factor, cross = lax.optimization_barrier((factor, cross))
    rows = panel_full.shape[0]
    inverse = lower_inverse(factor)
    solved = jnp.dot(jnp.concatenate([panel_full, cross], axis=0), inverse.T, precision=highest)
    orthonormal = solved[:rows]
    right_factor = solved[rows:]
    col_sumsq = gather_psum(jnp.sum(right_factor * right_factor, axis=0), "tensor", tensor_size)
    new_basis = right_factor / jnp.sqrt(col_sumsq + 1e-06)
    new_momentum = buffer - 0.1 * jnp.dot(orthonormal, right_factor.T, precision=highest)
    total_rows = buffer.shape[0] * lax.axis_size("fsdp")
    total_cols = buffer.shape[1] * lax.axis_size("tensor")
    step_scale = 0.2 * jnp.sqrt(jnp.float32(total_rows * total_cols / basis.shape[1]))
    update = jnp.dot(orthonormal, new_basis.T, precision=highest)
    new_weight = (weight.astype(jnp.float32) - step_scale * update).astype(jnp.bfloat16)
    return (new_momentum, new_basis, new_weight)


def solution(mesh):
    placed = (P("fsdp", "tensor"), P("fsdp", "tensor"), P("fsdp", "tensor"), P("tensor", None))
    return jax.shard_map(
        local,
        mesh=mesh,
        in_specs=placed,
        out_specs=(P("fsdp", "tensor"), P("tensor", None), P("fsdp", "tensor")),
        check_vma=False,
    )
```

```python
import jax
import jax.numpy as jnp
from jax import lax
from jax.sharding import PartitionSpec as P


def scatter_gather_psum(x, axis, size):
    chunks = x.reshape(size, -1, 128)
    mine = jnp.sum(lax.all_to_all(chunks, axis, 0, 0, tiled=False), axis=0)
    spread = jnp.broadcast_to(mine[None], chunks.shape)
    return lax.all_to_all(spread, axis, 0, 0, tiled=False).reshape(x.shape)


def padded_scatter_psum(x, axis, size):
    flat = x.reshape(-1)
    chunk = size * 8 * 128
    padded = jnp.pad(flat, (0, (-flat.shape[0]) % chunk))
    chunks = padded.reshape(size, -1, 128)
    return jnp.sum(lax.all_to_all(chunks, axis, 0, 0, tiled=False), axis=0)


def padded_gather(mine, axis, size, like):
    spread = jnp.broadcast_to(mine[None], (size,) + mine.shape)
    whole = lax.all_to_all(spread, axis, 0, 0, tiled=False).reshape(-1)
    return whole[: like.size].reshape(like.shape)


def lower_blocks(matrix, block):
    count = matrix.shape[0] // block
    return jnp.stack([matrix[i * block:(i + 1) * block, j * block:(j + 1) * block] for i in range(count) for j in range(i + 1)])


def symmetric_from_lower_blocks(blocks, count):
    block = blocks.shape[-1]
    index = {}
    for i in range(count):
        for j in range(i + 1):
            index[(i, j)] = len(index)
    rows = []
    for i in range(count):
        row = [blocks[index[(i, j)]] if j <= i else blocks[index[(j, i)]].T for j in range(count)]
        rows.append(jnp.concatenate(row, axis=1))
    return jnp.concatenate(rows, axis=0)


def lower_inverse(factor):
    leaf = 32
    levels = [factor[None]]
    while levels[-1].shape[-1] > leaf:
        blocks = levels[-1]
        half = blocks.shape[-1] // 2
        pair = jnp.stack([blocks[:, :half, :half], blocks[:, half:, half:]], axis=1)
        levels.append(pair.reshape(-1, half, half))
    unit = jnp.eye(leaf, dtype=factor.dtype)
    diagonal = jnp.sum(levels[-1] * unit, axis=2)
    strict = levels[-1] / diagonal[:, :, None] - unit
    inverse = unit - strict
    power = strict
    span = 2
    while span < leaf:
        power = jnp.matmul(power, power, precision=lax.Precision.HIGHEST)
        inverse = jnp.matmul(inverse, unit + power, precision=lax.Precision.HIGHEST)
        span *= 2
    inverse = inverse / diagonal[:, None, :]
    for blocks in reversed(levels[:-1]):
        width = blocks.shape[-1] // 2
        upper = inverse[0::2]
        lower = inverse[1::2]
        corner = blocks[:, width:, :width]
        off = -jnp.matmul(jnp.matmul(lower, corner, precision=lax.Precision.HIGHEST), upper, precision=lax.Precision.HIGHEST)
        top = jnp.concatenate([upper, jnp.zeros_like(upper)], axis=2)
        bottom = jnp.concatenate([off, lower], axis=2)
        inverse = jnp.concatenate([top, bottom], axis=1)
    return inverse[0]


def gather_psum(x, axis, size):
    copies = jnp.broadcast_to(x[None], (size,) + x.shape)
    return jnp.sum(lax.all_to_all(copies, axis, 0, 0, tiled=False), axis=0)


def local(momentum, gradient, weight, basis):
    highest = lax.Precision.HIGHEST
    rank = basis.shape[1]
    buffer = momentum + gradient.astype(jnp.float32)
    panel_part = jnp.dot(buffer, basis, precision=highest)
    tensor_size = lax.axis_size("tensor")
    panel_full = scatter_gather_psum(panel_part, "tensor", tensor_size)
    gram_part = jnp.dot(panel_full.T, panel_full, precision=highest)
    block = 128
    fsdp_size = lax.axis_size("fsdp")
    gram_lower = lower_blocks(gram_part, block)
    flat = gram_lower.reshape(-1)
    flat = jnp.pad(flat, (0, (-flat.shape[0]) % (tensor_size * 128)))
    share = lax.dynamic_index_in_dim(flat.reshape(tensor_size, -1, 128), lax.axis_index("tensor"), 0, keepdims=False)
    share = gather_psum(share, "fsdp", fsdp_size)
    shares = lax.all_to_all(jnp.broadcast_to(share[None], (tensor_size,) + share.shape), "tensor", 0, 0, tiled=False)
    gram_blocks = shares.reshape(-1)[: gram_lower.size].reshape(gram_lower.shape)
    cross_part, gram_blocks = lax.optimization_barrier((jnp.dot(buffer.T, panel_full, precision=highest), gram_blocks))
    cross_mine = padded_scatter_psum(cross_part, "fsdp", fsdp_size)
    gram_matrix = symmetric_from_lower_blocks(gram_blocks, rank // block)
    cross = padded_gather(cross_mine, "fsdp", fsdp_size, cross_part)
    factor = jnp.linalg.cholesky(gram_matrix)
    factor, cross = lax.optimization_barrier((factor, cross))
    rows = panel_full.shape[0]
    inverse = lower_inverse(factor)
    solved = jnp.dot(jnp.concatenate([panel_full, cross], axis=0), inverse.T, precision=highest)
    orthonormal = solved[:rows]
    right_factor = solved[rows:]
    col_sumsq = gather_psum(jnp.sum(right_factor * right_factor, axis=0), "tensor", tensor_size)
    new_basis = right_factor / jnp.sqrt(col_sumsq + 1e-06)
    new_momentum = buffer - 0.1 * jnp.dot(orthonormal, right_factor.T, precision=highest)
    total_rows = buffer.shape[0] * lax.axis_size("fsdp")
    total_cols = buffer.shape[1] * lax.axis_size("tensor")
    step_scale = 0.2 * jnp.sqrt(jnp.float32(total_rows * total_cols / basis.shape[1]))
    update = jnp.dot(orthonormal, new_basis.T, precision=highest)
    new_weight = (weight.astype(jnp.float32) - step_scale * update).astype(jnp.bfloat16)
    return (new_momentum, new_basis, new_weight)


def solution(mesh):
    placed = (P("fsdp", "tensor"), P("fsdp", "tensor"), P("fsdp", "tensor"), P("tensor", None))
    return jax.shard_map(
        local,
        mesh=mesh,
        in_specs=placed,
        out_specs=(P("fsdp", "tensor"), P("tensor", None), P("fsdp", "tensor")),
        check_vma=False,
    )
```
